128 devices in a mesh: grp: 4 (over y_lo, core), chan: 32 (over z, y_hi, x).
Axes of the slice: x: 4, y: 4 (y_hi: 2, y_lo: 2; y = y_hi * 2 + y_lo), z: 4, core: 2. Of those that a mesh axis runs over, the one named last changes fastest.
Arguments:
- voltages: bfloat16 [128, 2048, 128], P(None, ('grp', 'chan')), may hold values from -6 to 6
- model_vis: bfloat16 [128, 136, 2, 128, 128], P(('grp', 'chan')), may hold values from -1.1953125 to 1.1953125
- kernel_u: bfloat16 [128, 16, 128, 128], P(('grp', 'chan')), may hold values from -1.5 to 1.5
- kernel_v: bfloat16 [128, 16, 128, 128], P(('grp', 'chan')), may hold values from -1.5 to 1.5
- pair_slot: int32 [128, 136], P(('grp', 'chan')), may hold values from 0 to 15
- slot_block: int32 [128, 16], P(('grp', 'chan')), may hold values from 0 to 1023, as said below
- slot_count: int32 [128], P(('grp', 'chan')), may hold values from 8 to 16
Outputs:
- image: float32 [256, 2048], P('chan', 'grp')
The draws below stay inside these ranges and needn't reach their ends.
Inputs may be any that keep to these rules, and one draw needn't show every extreme that they name: `pair_slot`: pairs whose slot is at or above the channel's slot_count are not imaged. `slot_block`: the 16 block ids of one channel are distinct.
All inputs are finite; a program needn't handle non-finite values.
Results may differ from the reference program's by a relative error of at most 0.0049.
Values may be sent and summed in bfloat16 or wider, within the bound.
No kernel may reach another device: no remote copies, remote signals or barrier semaphores. Data moves between devices by JAX's collectives and lax.ppermute only.
A program may use at most 192 MiB of HBM per device.

```python
import jax
import jax.numpy as jnp
import numpy as np
from jax import lax

ANTENNAS = 2048
SAMPLES = 64
TILE = 128
BLOCK = 128
GRID = 4096
CROP = 2048
SLOTS = 16
ROWS = 256
TILES = 16
PAIRS = 136
BLOCKS = 1024
CHANNELS = 128


def draw_slot_count(key, part):
    counts = jax.random.randint(jax.random.fold_in(key, 3), (CHANNELS,), SLOTS // 2, SLOTS + 1)
    counts = counts.at[0].set(SLOTS)
    counts = counts.at[CHANNELS - 1].set(SLOTS // 2)
    return counts.astype(jnp.int32)


def draw_slot_block(key, part):
    scores = jax.random.randint(jax.random.fold_in(key, 5), (CHANNELS, BLOCKS), 0, 2 ** 20)
    row_index = jnp.arange(CHANNELS, dtype=jnp.int32)[:, None]
    col_index = jnp.arange(BLOCKS, dtype=jnp.int32)[None, :]
    ranking = scores * BLOCKS + col_index
    ranking = jnp.where((row_index == 0) & (col_index == BLOCKS - 1), -1, ranking)
    ranking = jnp.where((row_index == CHANNELS - 1) & (col_index == 0), -1, ranking)
    return jnp.argsort(ranking, axis=1)[:, :SLOTS].astype(jnp.int32)


def edge_profile(strength, reach):
    rows = jnp.arange(BLOCK, dtype=jnp.int32)
    depth = jnp.minimum(rows, BLOCK - 1 - rows).astype(jnp.float32)
    return (1.0 + strength * jnp.exp(-depth / reach)) / (1.0 + strength)


def draw_kernel_u(key, part):
    sub_key = jax.random.fold_in(key, 11)
    shape = (CHANNELS, TILES, BLOCK, TILE)
    base = jnp.clip(jax.random.normal(sub_key, shape, jnp.float32) / 3.0, -1.0, 1.0)
    profile = edge_profile(8.0, 2.0)
    return (1.5 * base * profile[None, None, :, None]).astype(jnp.bfloat16)


def draw_kernel_v(key, part):
    sub_key = jax.random.fold_in(key, 13)
    shape = (CHANNELS, TILES, BLOCK, TILE)
    base = jnp.clip(jax.random.normal(sub_key, shape, jnp.float32) / 3.0, -1.0, 1.0)
    profile = edge_profile(8.0, 2.0)
    return (1.5 * base * profile[None, None, :, None]).astype(jnp.bfloat16)


def set_ends(array, own_key, smallest, top_value):
    longest = array.shape.index(max(array.shape))
    spots = []
    for shift in (0, 1):
        where = [jax.random.randint(jax.random.fold_in(own_key, axis), (), 0, length) for axis, length in enumerate(array.shape)]
        where[longest] = (where[longest] + shift) % array.shape[longest]
        spots.append(tuple(where))
    return array.at[spots[0]].set(smallest).at[spots[1]].set(top_value)


def levels(own_key, extent, shards, smallest, top_value):
    def one(axis_at, shards_of):
        steps = jax.random.uniform(jax.random.fold_in(jax.random.fold_in(own_key, 6), axis_at), (shards_of,), jnp.float32, smallest / len(shards), top_value / len(shards))
        return jnp.repeat(jnp.exp(steps), extent[axis_at] // shards_of).reshape((-1,) + (1,) * (len(extent) - axis_at - 1))

    level = one(*shards[0])
    for cut in shards[1:]:
        level = level * one(*cut)
    return level


def bell_draw(stream_key, extent, width, bound, pieces=(), kind=jnp.bfloat16):
    values = jax.random.normal(stream_key, extent, jnp.float32) * width
    if len(pieces) > 0:
        values = levels(stream_key, extent, pieces, -0.22, 0.18) * values
    return jnp.clip(values, min=-bound, max=bound).astype(kind)


def setup_inputs(seed: int = 0) -> dict:
    key_of = jax.random.split(jax.random.key(seed), 8)
    return {
        "voltages": bell_draw(key_of[0], (CHANNELS, ANTENNAS, 2 * SAMPLES), 1.0, 6.0, ((1, 128),)),
        "model_vis": bell_draw(key_of[1], (CHANNELS, PAIRS, 2, TILE, TILE), 0.2, 1.1953125, ((0, 128),)),
        "kernel_u": draw_kernel_u(jax.random.fold_in(key_of[7], 71), 0),
        "kernel_v": draw_kernel_v(jax.random.fold_in(key_of[7], 71), 0),
        "pair_slot": set_ends(jax.random.randint(key_of[4], (CHANNELS, PAIRS), 0, SLOTS), jax.random.fold_in(key_of[4], 1), 0, SLOTS - 1).astype(jnp.int32),
        "slot_block": draw_slot_block(jax.random.fold_in(key_of[7], 71), 0),
        "slot_count": draw_slot_count(jax.random.fold_in(key_of[7], 71), 0),
    }


def grid_channel(antenna_volts, model_one, kernel_u_one, kernel_v_one, slots_one, count_one):
    row_tiles, col_tiles = np.triu_indices(TILES)
    antenna_tiles = antenna_volts.astype(jnp.float32).reshape(TILES, TILE, 2 * SAMPLES)
    swapped = jnp.concatenate([-antenna_tiles[:, :, SAMPLES:], antenna_tiles[:, :, :SAMPLES]], axis=2)
    row_volts = antenna_tiles[row_tiles]
    real_part = jnp.einsum("kat,kbt->kab", row_volts, antenna_tiles[col_tiles])
    imag_part = jnp.einsum("kat,kbt->kab", row_volts, swapped[col_tiles])
    gram_tiles = jnp.stack([real_part, imag_part], axis=1) / SAMPLES
    residual = (gram_tiles - model_one.astype(jnp.float32)).astype(jnp.bfloat16)
    half_grid = jnp.einsum("kua,kcab->kcub", kernel_u_one[row_tiles].astype(jnp.float32), residual.astype(jnp.float32)).astype(jnp.bfloat16)
    tile_grid = jnp.einsum("kcub,kvb->kucv", half_grid.astype(jnp.float32), kernel_v_one[col_tiles].astype(jnp.float32))
    live_mask = (slots_one < count_one).astype(jnp.float32)
    slot_onehot = (slots_one[:, None] == jnp.arange(SLOTS, dtype=jnp.int32)[None, :]).astype(jnp.float32) * live_mask[:, None]
    slot_grids = jnp.dot(slot_onehot.T, tile_grid.reshape(PAIRS, BLOCK * 2 * BLOCK), precision=lax.Precision.HIGHEST)
    return slot_grids.astype(jnp.bfloat16).reshape(SLOTS, BLOCK, 2, BLOCK)


def reference(voltages, model_vis, kernel_u, kernel_v, pair_slot, slot_block, slot_count):
    per_side = GRID // BLOCK

    def one_channel(uv_total, inputs):
        antenna_volts, model_one, kernel_u_one, kernel_v_one, slots_one, blocks_one, count_one = inputs
        slot_grids = grid_channel(antenna_volts, model_one, kernel_u_one, kernel_v_one, slots_one, count_one).astype(jnp.float32)

        def place_slot(slot_index, accumulated):
            block_id = blocks_one[slot_index]
            row_start = ((block_id // per_side) * BLOCK).astype(jnp.int32)
            col_start = ((block_id % per_side) * BLOCK).astype(jnp.int32)
            starts = (row_start, jnp.int32(0), col_start)
            current = lax.dynamic_slice(accumulated, starts, (BLOCK, 2, BLOCK))
            return lax.dynamic_update_slice(accumulated, current + slot_grids[slot_index], starts)

        return lax.fori_loop(0, SLOTS, place_slot, uv_total), None

    uv_total = jnp.zeros((GRID, 2, GRID), jnp.float32)
    uv_total, unused = lax.scan(one_channel, uv_total, (voltages, model_vis, kernel_u, kernel_v, pair_slot, slot_block, slot_count))
    uv_field = uv_total[:, 0, :] + 1j * uv_total[:, 1, :]
    sky_image = jnp.fft.fftshift(jnp.fft.ifft2(jnp.fft.ifftshift(uv_field))).real * GRID
    first_row = GRID // 2 - ROWS // 2
    first_col = GRID // 2 - CROP // 2
    return sky_image[first_row:first_row + ROWS, first_col:first_col + CROP].astype(jnp.float32)
```

```python
import math

import jax
import jax.numpy as jnp
import numpy as np
from jax import lax
from jax.experimental import pallas as pl
from jax.experimental.pallas import tpu as pltpu
from jax.sharding import PartitionSpec as P

ANTENNAS = 2048
SAMPLES = 64
TILE = 128
BLOCK = 128
GRID = 4096
CROP = 2048
SLOTS = 16
ROWS = 256
TILES = 16
PAIRS = 136
PHASES = 32

TWO_PI = 2.0 * math.pi


def _grid_kernel(ptab, qtab, slot_ref, count_ref, v_ref, s_ref, model_ref, ku_ref, kv_ref, out_ref, acc_ref):
    acc_ref[...] = jnp.zeros_like(acc_ref)
    count = count_ref[0]
    nt = (((1,), (1,)), ((), ()))

    def body(k, carry):
        p = ptab[k]
        q = qtab[k]
        slot = slot_ref[k]
        p0 = pl.multiple_of(p * TILE, TILE)
        q0 = pl.multiple_of(q * TILE, TILE)
        vp = v_ref[pl.ds(p0, TILE), :]
        vq = v_ref[pl.ds(q0, TILE), :]
        sq = s_ref[pl.ds(q0, TILE), :]
        rhs = jnp.concatenate([vq, sq], axis=0)
        gram = lax.dot_general(vp, rhs, nt, preferred_element_type=jnp.float32)
        model = jnp.concatenate([model_ref[k, 0], model_ref[k, 1]], axis=1).astype(jnp.float32)
        residual = (gram * (1.0 / SAMPLES) - model).astype(jnp.bfloat16)
        half = jnp.dot(ku_ref[p], residual, preferred_element_type=jnp.float32).astype(jnp.bfloat16)
        half_rows = jnp.concatenate([half[:, :TILE], half[:, TILE:]], axis=0)
        tile = lax.dot_general(half_rows, kv_ref[q], nt, preferred_element_type=jnp.float32)
        live = (slot < count) & (slot >= 0)
        slot_c = jnp.clip(slot, 0, SLOTS - 1)

        @pl.when(live)
        def _():
            acc_ref[slot_c] += tile

        return carry

    lax.fori_loop(0, PAIRS, body, 0)
    out_ref[...] = acc_ref[...].astype(out_ref.dtype)


def grid_slots(antenna_volts, model_one, kernel_u_one, kernel_v_one, slots_one, count_one):
    row_tiles, col_tiles = np.triu_indices(TILES)
    ptab = jnp.asarray(row_tiles, jnp.int32)
    qtab = jnp.asarray(col_tiles, jnp.int32)
    swapped = jnp.concatenate([-antenna_volts[:, SAMPLES:], antenna_volts[:, :SAMPLES]], axis=1)
    smem = pl.BlockSpec(memory_space=pltpu.SMEM)
    vmem = pl.BlockSpec(memory_space=pltpu.VMEM)
    flops = PAIRS * 3 * 2 * (2 * TILE) * TILE * TILE
    return pl.pallas_call(
        _grid_kernel,
        out_shape=jax.ShapeDtypeStruct((SLOTS, 2 * BLOCK, BLOCK), jnp.bfloat16),
        in_specs=[smem, smem, smem, smem, vmem, vmem, vmem, vmem, vmem],
        out_specs=vmem,
        scratch_shapes=[pltpu.VMEM((SLOTS, 2 * BLOCK, BLOCK), jnp.float32)],
        compiler_params=pltpu.CompilerParams(vmem_limit_bytes=48 * 1024 * 1024),
        cost_estimate=pl.CostEstimate(flops=flops, transcendentals=0, bytes_accessed=11 * 1024 * 1024),
    )(ptab, qtab, slots_one, count_one, antenna_volts, swapped, model_one, kernel_u_one, kernel_v_one)


def _cos_sin(index, period):
    angles = index.astype(jnp.float32) * (TWO_PI / period)
    return jnp.cos(angles), jnp.sin(angles)


def channel_image(slot_grids, blocks_here):
    per_side = GRID // BLOCK
    grids = slot_grids.reshape(SLOTS, 2, BLOCK, BLOCK).astype(jnp.float32)
    block_rows = blocks_here // per_side
    block_cols = blocks_here % per_side
    offsets = jnp.arange(BLOCK, dtype=jnp.int32)
    pixel_rows = jnp.arange(ROWS, dtype=jnp.int32) - ROWS // 2
    grid_rows = block_rows[:, None] * BLOCK + offsets[None, :] - GRID // 2
    ar, ai = _cos_sin(jnp.mod(pixel_rows[None, :, None] * grid_rows[:, None, :], GRID), GRID)
    row_op = jnp.stack([jnp.stack([ar, -ai], axis=2), jnp.stack([ai, ar], axis=2)], axis=1)
    rows_done = jnp.einsum(
        "sclku,skuv->sclv", row_op, grids, precision=lax.Precision.HIGH, preferred_element_type=jnp.float32
    )
    phases = jnp.arange(PHASES, dtype=jnp.int32)
    zr, zi = _cos_sin(jnp.mod(phases[:, None] * block_cols[None, :], PHASES), PHASES)
    phase_op = jnp.stack([jnp.stack([zr, -zi], axis=2), jnp.stack([zi, zr], axis=2)], axis=1)
    summed = jnp.einsum(
        "tcsk,sklv->tclv", phase_op, rows_done, precision=lax.Precision.HIGH, preferred_element_type=jnp.float32
    )
    col_groups = jnp.arange(CROP // PHASES, dtype=jnp.int32)
    pixel_cols = col_groups[None, :] * PHASES + phases[:, None] - CROP // 2
    br, bi = _cos_sin(jnp.mod(pixel_cols[:, None, :] * (offsets - GRID // 2)[None, :, None], GRID), GRID)
    col_op = jnp.stack([br, -bi], axis=1)
    return jnp.einsum(
        "tclv,tcvj->tlj", summed, col_op, precision=lax.Precision.HIGH, preferred_element_type=jnp.float32
    ) * (1.0 / GRID)


def body(voltages, model_vis, kernel_u, kernel_v, pair_slot, slot_block, slot_count):
    local_antennas = voltages.shape[1]
    direct = voltages.reshape(voltages.shape[0], 1, local_antennas, 2 * SAMPLES)
    turned = lax.all_to_all(direct, ("grp", "chan"), split_axis=0, concat_axis=1, tiled=True)
    antenna_volts = turned.reshape(ANTENNAS, 2 * SAMPLES)
    slot_grids = grid_slots(
        antenna_volts, model_vis[0], kernel_u[0], kernel_v[0], pair_slot[0], slot_count
    )
    image_t = channel_image(slot_grids, slot_block[0])
    n_chan = lax.axis_size("chan")
    n_grp = lax.axis_size("grp")
    rows_per = ROWS // n_chan
    groups_per = CROP // PHASES // n_grp
    send = image_t.reshape(PHASES, n_chan, rows_per, n_grp, groups_per).transpose(1, 3, 2, 4, 0)
    send = send.reshape(n_chan * n_grp, rows_per, groups_per, PHASES)
    got = lax.all_to_all(send, ("chan", "grp"), split_axis=0, concat_axis=0, tiled=True)
    return got.sum(axis=0).reshape(rows_per, groups_per * PHASES)


def solution(mesh):
    in_specs = (
        P(None, ("grp", "chan"), None),
        P(("grp", "chan"), None, None, None, None),
        P(("grp", "chan"), None, None, None),
        P(("grp", "chan"), None, None, None),
        P(("grp", "chan"), None),
        P(("grp", "chan"), None),
        P(("grp", "chan")),
    )
    out_specs = P("chan", "grp")
    return jax.shard_map(body, mesh=mesh, in_specs=in_specs, out_specs=out_specs, check_vma=False)
```

```python
import math

import jax
import jax.numpy as jnp
import numpy as np
from jax import lax
from jax.experimental import pallas as pl
from jax.experimental.pallas import tpu as pltpu
from jax.sharding import PartitionSpec as P

ANTENNAS = 2048
SAMPLES = 64
TILE = 128
BLOCK = 128
GRID = 4096
CROP = 2048
SLOTS = 16
ROWS = 256
TILES = 16
PAIRS = 136
PHASES = 32

TWO_PI = 2.0 * math.pi


def _grid_kernel(ptab, qtab, slot_ref, count_ref, v_ref, w_ref, model_ref, ku_ref, kvt_ref, out_ref, acc_ref):
    acc_ref[...] = jnp.zeros_like(acc_ref)
    count = count_ref[0]

    def body(k, carry):
        p = ptab[k]
        q = qtab[k]
        slot = slot_ref[k]
        gram = jnp.dot(v_ref[p], w_ref[q], preferred_element_type=jnp.float32)
        model = jnp.concatenate([model_ref[k, 0], model_ref[k, 1]], axis=1).astype(jnp.float32)
        residual = (gram * (1.0 / SAMPLES) - model).astype(jnp.bfloat16)
        half = jnp.dot(ku_ref[p], residual, preferred_element_type=jnp.float32).astype(jnp.bfloat16)
        half_rows = jnp.concatenate([half[:, :TILE], half[:, TILE:]], axis=0)
        tile = jnp.dot(half_rows, kvt_ref[q], preferred_element_type=jnp.float32)
        live = (slot < count) & (slot >= 0)
        slot_c = jnp.clip(slot, 0, SLOTS - 1)

        @pl.when(live)
        def _():
            acc_ref[slot_c] += tile

        return carry

    lax.fori_loop(0, PAIRS, body, 0, unroll=4)
    out_ref[...] = acc_ref[...].astype(out_ref.dtype)


def grid_slots(antenna_volts, model_one, kernel_u_one, kernel_v_one, slots_one, count_one):
    row_tiles, col_tiles = np.triu_indices(TILES)
    ptab = jnp.asarray(row_tiles, jnp.int32)
    qtab = jnp.asarray(col_tiles, jnp.int32)
    swapped = jnp.concatenate([-antenna_volts[:, SAMPLES:], antenna_volts[:, :SAMPLES]], axis=1)
    tiles = antenna_volts.reshape(TILES, TILE, 2 * SAMPLES)
    turned = jnp.concatenate(
        [tiles.transpose(0, 2, 1), swapped.reshape(TILES, TILE, 2 * SAMPLES).transpose(0, 2, 1)], axis=2
    )
    kv_turned = kernel_v_one.transpose(0, 2, 1)
    smem = pl.BlockSpec(memory_space=pltpu.SMEM)
    vmem = pl.BlockSpec(memory_space=pltpu.VMEM)
    flops = PAIRS * 3 * 2 * (2 * TILE) * TILE * TILE
    return pl.pallas_call(
        _grid_kernel,
        out_shape=jax.ShapeDtypeStruct((SLOTS, 2 * BLOCK, BLOCK), jnp.bfloat16),
        in_specs=[smem, smem, smem, smem, vmem, vmem, vmem, vmem, vmem],
        out_specs=vmem,
        scratch_shapes=[pltpu.VMEM((SLOTS, 2 * BLOCK, BLOCK), jnp.float32)],
        compiler_params=pltpu.CompilerParams(vmem_limit_bytes=48 * 1024 * 1024),
        cost_estimate=pl.CostEstimate(flops=flops, transcendentals=0, bytes_accessed=11 * 1024 * 1024),
    )(ptab, qtab, slots_one, count_one, tiles, turned, model_one, kernel_u_one, kv_turned)


def _cos_sin(index, period):
    angles = index.astype(jnp.float32) * (TWO_PI / period)
    return jnp.cos(angles), jnp.sin(angles)


def channel_image(slot_grids, blocks_here):
    per_side = GRID // BLOCK
    grids = slot_grids.reshape(SLOTS, 2, BLOCK, BLOCK).astype(jnp.float32)
    block_rows = blocks_here // per_side
    block_cols = blocks_here % per_side
    offsets = jnp.arange(BLOCK, dtype=jnp.int32)
    pixel_rows = jnp.arange(ROWS, dtype=jnp.int32) - ROWS // 2
    grid_rows = block_rows[:, None] * BLOCK + offsets[None, :] - GRID // 2
    ar, ai = _cos_sin(jnp.mod(pixel_rows[None, :, None] * grid_rows[:, None, :], GRID), GRID)
    row_op = jnp.stack([jnp.stack([ar, -ai], axis=2), jnp.stack([ai, ar], axis=2)], axis=1)
    rows_done = jnp.einsum(
        "sclku,skuv->sclv", row_op, grids, precision=lax.Precision.HIGH, preferred_element_type=jnp.float32
    )
    phases = jnp.arange(PHASES, dtype=jnp.int32)
    zr, zi = _cos_sin(jnp.mod(phases[:, None] * block_cols[None, :], PHASES), PHASES)
    phase_op = jnp.stack([jnp.stack([zr, -zi], axis=2), jnp.stack([zi, zr], axis=2)], axis=1)
    summed = jnp.einsum(
        "tcsk,sklv->tclv", phase_op, rows_done, precision=lax.Precision.HIGH, preferred_element_type=jnp.float32
    )
    col_groups = jnp.arange(CROP // PHASES, dtype=jnp.int32)
    pixel_cols = col_groups[None, :] * PHASES + phases[:, None] - CROP // 2
    br, bi = _cos_sin(jnp.mod(pixel_cols[:, None, :] * (offsets - GRID // 2)[None, :, None], GRID), GRID)
    col_op = jnp.stack([br, -bi], axis=1)
    return jnp.einsum(
        "tclv,tcvj->tlj", summed, col_op, precision=lax.Precision.HIGH, preferred_element_type=jnp.float32
    ) * (1.0 / GRID)


def body(voltages, model_vis, kernel_u, kernel_v, pair_slot, slot_block, slot_count):
    local_antennas = voltages.shape[1]
    direct = voltages.reshape(voltages.shape[0], 1, local_antennas, 2 * SAMPLES)
    turned = lax.all_to_all(direct, ("grp", "chan"), split_axis=0, concat_axis=1, tiled=True)
    antenna_volts = turned.reshape(ANTENNAS, 2 * SAMPLES)
    slot_grids = grid_slots(
        antenna_volts, model_vis[0], kernel_u[0], kernel_v[0], pair_slot[0], slot_count
    )
    image_t = channel_image(slot_grids, slot_block[0])
    n_chan = lax.axis_size("chan")
    n_grp = lax.axis_size("grp")
    rows_per = ROWS // n_chan
    groups_per = CROP // PHASES // n_grp
    send = image_t.reshape(PHASES, n_chan, rows_per, n_grp, groups_per).transpose(1, 3, 0, 2, 4)
    send = send.reshape(n_chan * n_grp, PHASES * rows_per * groups_per)
    got = lax.all_to_all(send, ("chan", "grp"), split_axis=0, concat_axis=0, tiled=True)
    summed = got.sum(axis=0).reshape(PHASES, rows_per, groups_per)
    return summed.transpose(1, 2, 0).reshape(rows_per, groups_per * PHASES)


def solution(mesh):
    in_specs = (
        P(None, ("grp", "chan"), None),
        P(("grp", "chan"), None, None, None, None),
        P(("grp", "chan"), None, None, None),
        P(("grp", "chan"), None, None, None),
        P(("grp", "chan"), None),
        P(("grp", "chan"), None),
        P(("grp", "chan")),
    )
    out_specs = P("chan", "grp")
    return jax.shard_map(body, mesh=mesh, in_specs=in_specs, out_specs=out_specs, check_vma=False)
```

```python
import math

import jax
import jax.numpy as jnp
import numpy as np
from jax import lax
from jax.experimental import pallas as pl
from jax.experimental.pallas import tpu as pltpu
from jax.sharding import PartitionSpec as P

ANTENNAS = 2048
SAMPLES = 64
TILE = 128
BLOCK = 128
GRID = 4096
CROP = 2048
SLOTS = 16
ROWS = 256
TILES = 16
PAIRS = 136
PHASES = 32

TWO_PI = 2.0 * math.pi


def _grid_kernel(ptab, qtab, slot_ref, count_ref, v_ref, w_ref, model_ref, ku_ref, kvt_ref, out_ref, acc_ref):
    acc_ref[...] = jnp.zeros_like(acc_ref)
    count = count_ref[0]

    def body(k, carry):
        p = ptab[k]
        q = qtab[k]
        slot = slot_ref[k]
        gram = jnp.dot(v_ref[p], w_ref[q], preferred_element_type=jnp.float32)
        model = jnp.concatenate([model_ref[k, 0], model_ref[k, 1]], axis=1).astype(jnp.float32)
        residual = (gram * (1.0 / SAMPLES) - model).astype(jnp.bfloat16)
        half = jnp.dot(ku_ref[p], residual, preferred_element_type=jnp.float32).astype(jnp.bfloat16)
        half_rows = jnp.concatenate([half[:, :TILE], half[:, TILE:]], axis=0)
        tile = jnp.dot(half_rows, kvt_ref[q], preferred_element_type=jnp.float32)
        live = (slot < count) & (slot >= 0)
        slot_c = jnp.clip(slot, 0, SLOTS - 1)

        acc_ref[slot_c] += jnp.where(live, tile, 0.0)
        return carry

    lax.fori_loop(0, PAIRS, body, 0, unroll=8)
    out_ref[...] = acc_ref[...].astype(out_ref.dtype)


def grid_slots(antenna_volts, model_one, kernel_u_one, kernel_v_one, slots_one, count_one):
    row_tiles, col_tiles = np.triu_indices(TILES)
    ptab = jnp.asarray(row_tiles, jnp.int32)
    qtab = jnp.asarray(col_tiles, jnp.int32)
    swapped = jnp.concatenate([-antenna_volts[:, SAMPLES:], antenna_volts[:, :SAMPLES]], axis=1)
    tiles = antenna_volts.reshape(TILES, TILE, 2 * SAMPLES)
    turned = jnp.concatenate(
        [tiles.transpose(0, 2, 1), swapped.reshape(TILES, TILE, 2 * SAMPLES).transpose(0, 2, 1)], axis=2
    )
    kv_turned = kernel_v_one.transpose(0, 2, 1)
    smem = pl.BlockSpec(memory_space=pltpu.SMEM)
    vmem = pl.BlockSpec(memory_space=pltpu.VMEM)
    flops = PAIRS * 3 * 2 * (2 * TILE) * TILE * TILE
    return pl.pallas_call(
        _grid_kernel,
        out_shape=jax.ShapeDtypeStruct((SLOTS, 2 * BLOCK, BLOCK), jnp.bfloat16),
        in_specs=[smem, smem, smem, smem, vmem, vmem, vmem, vmem, vmem],
        out_specs=vmem,
        scratch_shapes=[pltpu.VMEM((SLOTS, 2 * BLOCK, BLOCK), jnp.float32)],
        compiler_params=pltpu.CompilerParams(vmem_limit_bytes=48 * 1024 * 1024),
        cost_estimate=pl.CostEstimate(flops=flops, transcendentals=0, bytes_accessed=11 * 1024 * 1024),
    )(ptab, qtab, slots_one, count_one, tiles, turned, model_one, kernel_u_one, kv_turned)


def _cos_sin(index, period):
    angles = index.astype(jnp.float32) * (TWO_PI / period)
    return jnp.cos(angles), jnp.sin(angles)


def channel_image(slot_grids, blocks_here):
    per_side = GRID // BLOCK
    grids = slot_grids.reshape(SLOTS, 2, BLOCK, BLOCK).astype(jnp.float32)
    block_rows = blocks_here // per_side
    block_cols = blocks_here % per_side
    offsets = jnp.arange(BLOCK, dtype=jnp.int32)
    pixel_rows = jnp.arange(ROWS, dtype=jnp.int32) - ROWS // 2
    grid_rows = block_rows[:, None] * BLOCK + offsets[None, :] - GRID // 2
    ar, ai = _cos_sin(jnp.mod(pixel_rows[None, :, None] * grid_rows[:, None, :], GRID), GRID)
    row_op = jnp.stack([jnp.stack([ar, -ai], axis=2), jnp.stack([ai, ar], axis=2)], axis=1)
    rows_done = jnp.einsum(
        "sclku,skuv->sclv", row_op, grids, precision=lax.Precision.HIGH, preferred_element_type=jnp.float32
    )
    phases = jnp.arange(PHASES, dtype=jnp.int32)
    zr, zi = _cos_sin(jnp.mod(phases[:, None] * block_cols[None, :], PHASES), PHASES)
    phase_op = jnp.stack([jnp.stack([zr, -zi], axis=2), jnp.stack([zi, zr], axis=2)], axis=1)
    summed = jnp.einsum(
        "tcsk,sklv->tclv", phase_op, rows_done, precision=lax.Precision.HIGH, preferred_element_type=jnp.float32
    )
    col_groups = jnp.arange(CROP // PHASES, dtype=jnp.int32)
    pixel_cols = col_groups[None, :] * PHASES + phases[:, None] - CROP // 2
    br, bi = _cos_sin(jnp.mod(pixel_cols[:, None, :] * (offsets - GRID // 2)[None, :, None], GRID), GRID)
    col_op = jnp.stack([br, -bi], axis=1)
    return jnp.einsum(
        "tclv,tcvj->tlj", summed, col_op, precision=lax.Precision.HIGH, preferred_element_type=jnp.float32
    ) * (1.0 / GRID)


def body(voltages, model_vis, kernel_u, kernel_v, pair_slot, slot_block, slot_count):
    local_antennas = voltages.shape[1]
    direct = voltages.reshape(voltages.shape[0], 1, local_antennas, 2 * SAMPLES)
    turned = lax.all_to_all(direct, ("grp", "chan"), split_axis=0, concat_axis=1, tiled=True)
    antenna_volts = turned.reshape(ANTENNAS, 2 * SAMPLES)
    slot_grids = grid_slots(
        antenna_volts, model_vis[0], kernel_u[0], kernel_v[0], pair_slot[0], slot_count
    )
    image_t = channel_image(slot_grids, slot_block[0])
    n_chan = lax.axis_size("chan")
    n_grp = lax.axis_size("grp")
    rows_per = ROWS // n_chan
    groups_per = CROP // PHASES // n_grp
    send = image_t.reshape(PHASES, n_chan, rows_per, n_grp, groups_per).transpose(1, 3, 0, 2, 4)
    send = send.reshape(n_chan * n_grp, PHASES * rows_per * groups_per)
    got = lax.all_to_all(send, ("chan", "grp"), split_axis=0, concat_axis=0, tiled=True)
    summed = got.sum(axis=0).reshape(PHASES, rows_per, groups_per)
    return summed.transpose(1, 2, 0).reshape(rows_per, groups_per * PHASES)


def solution(mesh):
    in_specs = (
        P(None, ("grp", "chan"), None),
        P(("grp", "chan"), None, None, None, None),
        P(("grp", "chan"), None, None, None),
        P(("grp", "chan"), None, None, None),
        P(("grp", "chan"), None),
        P(("grp", "chan"), None),
        P(("grp", "chan")),
    )
    out_specs = P("chan", "grp")
    return jax.shard_map(body, mesh=mesh, in_specs=in_specs, out_specs=out_specs, check_vma=False)
```

```python
import math

import jax
import jax.numpy as jnp
import numpy as np
from jax import lax
from jax.experimental import pallas as pl
from jax.experimental.pallas import tpu as pltpu
from jax.sharding import PartitionSpec as P

ANTENNAS = 2048
SAMPLES = 64
TILE = 128
BLOCK = 128
GRID = 4096
CROP = 2048
SLOTS = 16
ROWS = 256
TILES = 16
PAIRS = 136
PHASES = 32

TWO_PI = 2.0 * math.pi


def _grid_kernel(ptab, qtab, slot_ref, count_ref, v_ref, w_ref, model_ref, ku_ref, kvt_ref, out_ref, acc_ref):
    acc_ref[...] = jnp.zeros_like(acc_ref)
    count = count_ref[0]

    def body(k, carry):
        p = ptab[k]
        q = qtab[k]
        slot = slot_ref[k]
        gram = jnp.dot(v_ref[p], w_ref[q], preferred_element_type=jnp.float32)
        model = jnp.concatenate([model_ref[k, 0], model_ref[k, 1]], axis=1).astype(jnp.float32)
        residual = (gram * (1.0 / SAMPLES) - model).astype(jnp.bfloat16)
        half = jnp.dot(ku_ref[p], residual, preferred_element_type=jnp.float32).astype(jnp.bfloat16)
        half_rows = jnp.concatenate([half[:, :TILE], half[:, TILE:]], axis=0)
        tile = jnp.dot(half_rows, kvt_ref[q], preferred_element_type=jnp.float32)
        live = (slot < count) & (slot >= 0)
        slot_c = jnp.clip(slot, 0, SLOTS - 1)

        acc_ref[slot_c] += jnp.where(live, tile, 0.0)
        return carry

    lax.fori_loop(0, PAIRS, body, 0, unroll=8)
    out_ref[...] = acc_ref[...].astype(out_ref.dtype)


def grid_slots(antenna_volts, model_one, kernel_u_one, kernel_v_one, slots_one, count_one):
    row_tiles, col_tiles = np.triu_indices(TILES)
    ptab = jnp.asarray(row_tiles, jnp.int32)
    qtab = jnp.asarray(col_tiles, jnp.int32)
    swapped = jnp.concatenate([-antenna_volts[:, SAMPLES:], antenna_volts[:, :SAMPLES]], axis=1)
    tiles = antenna_volts.reshape(TILES, TILE, 2 * SAMPLES)
    turned = jnp.concatenate(
        [tiles.transpose(0, 2, 1), swapped.reshape(TILES, TILE, 2 * SAMPLES).transpose(0, 2, 1)], axis=2
    )
    kv_turned = kernel_v_one.transpose(0, 2, 1)
    smem = pl.BlockSpec(memory_space=pltpu.SMEM)
    vmem = pl.BlockSpec(memory_space=pltpu.VMEM)
    flops = PAIRS * 3 * 2 * (2 * TILE) * TILE * TILE
    return pl.pallas_call(
        _grid_kernel,
        out_shape=jax.ShapeDtypeStruct((SLOTS, 2 * BLOCK, BLOCK), jnp.bfloat16),
        in_specs=[smem, smem, smem, smem, vmem, vmem, vmem, vmem, vmem],
        out_specs=vmem,
        scratch_shapes=[pltpu.VMEM((SLOTS, 2 * BLOCK, BLOCK), jnp.float32)],
        compiler_params=pltpu.CompilerParams(vmem_limit_bytes=48 * 1024 * 1024),
        cost_estimate=pl.CostEstimate(flops=flops, transcendentals=0, bytes_accessed=11 * 1024 * 1024),
    )(ptab, qtab, slots_one, count_one, tiles, turned, model_one, kernel_u_one, kv_turned)


def _cos_sin(index, period):
    angles = index.astype(jnp.float32) * (TWO_PI / period)
    return jnp.cos(angles), jnp.sin(angles)


def channel_image(slot_grids, blocks_here):
    per_side = GRID // BLOCK
    grids = slot_grids.reshape(SLOTS, 2, BLOCK, BLOCK).astype(jnp.float32)
    block_rows = blocks_here // per_side
    block_cols = blocks_here % per_side
    offsets = jnp.arange(BLOCK, dtype=jnp.int32)
    pixel_rows = jnp.arange(ROWS, dtype=jnp.int32) - ROWS // 2
    grid_rows = block_rows[:, None] * BLOCK + offsets[None, :] - GRID // 2
    ar, ai = _cos_sin(jnp.mod(pixel_rows[None, :, None] * grid_rows[:, None, :], GRID), GRID)
    row_op = jnp.stack([jnp.stack([ar, -ai], axis=2), jnp.stack([ai, ar], axis=2)], axis=1)
    rows_done = jnp.einsum(
        "sclku,skuv->sclv", row_op, grids, precision=lax.Precision.HIGH, preferred_element_type=jnp.float32
    )
    phases = jnp.arange(PHASES, dtype=jnp.int32)
    zr, zi = _cos_sin(jnp.mod(phases[:, None] * block_cols[None, :], PHASES), PHASES)
    phase_op = jnp.stack([jnp.stack([zr, -zi], axis=2), jnp.stack([zi, zr], axis=2)], axis=1)
    summed = jnp.einsum(
        "tcsk,sklv->tclv", phase_op, rows_done, precision=lax.Precision.HIGH, preferred_element_type=jnp.float32
    )
    col_groups = jnp.arange(CROP // PHASES, dtype=jnp.int32)
    pixel_cols = col_groups[None, :] * PHASES + phases[:, None] - CROP // 2
    br, bi = _cos_sin(jnp.mod(pixel_cols[:, None, :] * (offsets - GRID // 2)[None, :, None], GRID), GRID)
    col_op = jnp.stack([br, -bi], axis=1)
    return jnp.einsum(
        "tclv,tcvj->tlj", summed, col_op, precision=lax.Precision.HIGH, preferred_element_type=jnp.float32
    ) * (1.0 / GRID)


def body(voltages, model_vis, kernel_u, kernel_v, pair_slot, slot_block, slot_count):
    local_antennas = voltages.shape[1]
    direct = voltages.reshape(voltages.shape[0], 1, local_antennas, 2 * SAMPLES)
    turned = lax.all_to_all(direct, ("grp", "chan"), split_axis=0, concat_axis=1, tiled=True)
    antenna_volts = turned.reshape(ANTENNAS, 2 * SAMPLES)
    slot_grids = grid_slots(
        antenna_volts, model_vis[0], kernel_u[0], kernel_v[0], pair_slot[0], slot_count
    )
    image_t = channel_image(slot_grids, slot_block[0])
    n_chan = lax.axis_size("chan")
    n_grp = lax.axis_size("grp")
    rows_per = ROWS // n_chan
    groups_per = CROP // PHASES // n_grp
    send = image_t.reshape(PHASES, n_chan, rows_per, n_grp, groups_per).transpose(1, 3, 0, 2, 4)
    send = send.reshape(n_chan * n_grp, PHASES * rows_per * groups_per).astype(jnp.bfloat16)
    got = lax.all_to_all(send, ("chan", "grp"), split_axis=0, concat_axis=0, tiled=True)
    summed = got.astype(jnp.float32).sum(axis=0).reshape(PHASES, rows_per, groups_per)
    return summed.transpose(1, 2, 0).reshape(rows_per, groups_per * PHASES)


def solution(mesh):
    in_specs = (
        P(None, ("grp", "chan"), None),
        P(("grp", "chan"), None, None, None, None),
        P(("grp", "chan"), None, None, None),
        P(("grp", "chan"), None, None, None),
        P(("grp", "chan"), None),
        P(("grp", "chan"), None),
        P(("grp", "chan")),
    )
    out_specs = P("chan", "grp")
    return jax.shard_map(body, mesh=mesh, in_specs=in_specs, out_specs=out_specs, check_vma=False)
```

```python
import math

import jax
import jax.numpy as jnp
import numpy as np
from jax import lax
from jax.experimental import pallas as pl
from jax.experimental.pallas import tpu as pltpu
from jax.sharding import PartitionSpec as P

ANTENNAS = 2048
SAMPLES = 64
TILE = 128
BLOCK = 128
GRID = 4096
CROP = 2048
SLOTS = 16
ROWS = 256
TILES = 16
PAIRS = 136
PHASES = 32

TWO_PI = 2.0 * math.pi


def _grid_kernel(ptab, qtab, slot_ref, count_ref, v_ref, w_ref, model_ref, ku_ref, kvt_ref, out_ref, acc_ref):
    acc_ref[...] = jnp.zeros_like(acc_ref)
    count = count_ref[0]

    def body(k, carry):
        p = ptab[k]
        q = qtab[k]
        slot = slot_ref[k]
        gram = jnp.dot(v_ref[p], w_ref[q], preferred_element_type=jnp.float32)
        model = jnp.concatenate([model_ref[k, 0], model_ref[k, 1]], axis=1).astype(jnp.float32)
        residual = (gram * (1.0 / SAMPLES) - model).astype(jnp.bfloat16)
        half = jnp.dot(ku_ref[p], residual, preferred_element_type=jnp.float32).astype(jnp.bfloat16)
        half_rows = jnp.concatenate([half[:, :TILE], half[:, TILE:]], axis=0)
        tile = jnp.dot(half_rows, kvt_ref[q], preferred_element_type=jnp.float32)
        live = (slot < count) & (slot >= 0)
        slot_c = jnp.clip(slot, 0, SLOTS - 1)

        acc_ref[slot_c] += jnp.where(live, tile, 0.0)
        return carry

    lax.fori_loop(0, PAIRS, body, 0, unroll=8)
    out_ref[...] = acc_ref[...].astype(out_ref.dtype)


def grid_slots(antenna_volts, model_one, kernel_u_one, kernel_v_one, slots_one, count_one):
    row_tiles, col_tiles = np.triu_indices(TILES)
    ptab = jnp.asarray(row_tiles, jnp.int32)
    qtab = jnp.asarray(col_tiles, jnp.int32)
    swapped = jnp.concatenate([-antenna_volts[:, SAMPLES:], antenna_volts[:, :SAMPLES]], axis=1)
    tiles = antenna_volts.reshape(TILES, TILE, 2 * SAMPLES)
    turned = jnp.concatenate(
        [tiles.transpose(0, 2, 1), swapped.reshape(TILES, TILE, 2 * SAMPLES).transpose(0, 2, 1)], axis=2
    )
    kv_turned = kernel_v_one.transpose(0, 2, 1)
    smem = pl.BlockSpec(memory_space=pltpu.SMEM)
    vmem = pl.BlockSpec(memory_space=pltpu.VMEM)
    flops = PAIRS * 3 * 2 * (2 * TILE) * TILE * TILE
    return pl.pallas_call(
        _grid_kernel,
        out_shape=jax.ShapeDtypeStruct((SLOTS, 2 * BLOCK, BLOCK), jnp.bfloat16),
        in_specs=[smem, smem, smem, smem, vmem, vmem, vmem, vmem, vmem],
        out_specs=vmem,
        scratch_shapes=[pltpu.VMEM((SLOTS, 2 * BLOCK, BLOCK), jnp.float32)],
        compiler_params=pltpu.CompilerParams(vmem_limit_bytes=48 * 1024 * 1024),
        cost_estimate=pl.CostEstimate(flops=flops, transcendentals=0, bytes_accessed=11 * 1024 * 1024),
    )(ptab, qtab, slots_one, count_one, tiles, turned, model_one, kernel_u_one, kv_turned)


def _cos_sin(index, period):
    angles = index.astype(jnp.float32) * (TWO_PI / period)
    return jnp.cos(angles), jnp.sin(angles)


def channel_image(slot_grids, blocks_here):
    per_side = GRID // BLOCK
    grids = slot_grids.reshape(SLOTS, 2, BLOCK, BLOCK).astype(jnp.float32)
    block_rows = blocks_here // per_side
    block_cols = blocks_here % per_side
    offsets = jnp.arange(BLOCK, dtype=jnp.int32)
    pixel_rows = jnp.arange(ROWS, dtype=jnp.int32) - ROWS // 2
    grid_rows = block_rows[:, None] * BLOCK + offsets[None, :] - GRID // 2
    ar, ai = _cos_sin(jnp.mod(pixel_rows[None, :, None] * grid_rows[:, None, :], GRID), GRID)
    row_op = jnp.stack([jnp.stack([ar, -ai], axis=2), jnp.stack([ai, ar], axis=2)], axis=1)
    rows_done = jnp.einsum(
        "sclku,skuv->sclv", row_op, grids, precision=lax.Precision.HIGH, preferred_element_type=jnp.float32
    )
    phases = jnp.arange(PHASES, dtype=jnp.int32)
    zr, zi = _cos_sin(jnp.mod(phases[:, None] * block_cols[None, :], PHASES), PHASES)
    phase_op = jnp.stack([jnp.stack([zr, -zi], axis=2), jnp.stack([zi, zr], axis=2)], axis=1)
    summed = jnp.einsum(
        "tcsk,sklv->ltcv", phase_op, rows_done, precision=lax.Precision.HIGH, preferred_element_type=jnp.float32
    )
    dr, di = _cos_sin(jnp.mod((phases[:, None] - GRID // 4) * offsets[None, :] - (GRID // 2) * phases[:, None], GRID), GRID)
    turned_r = summed[:, :, 0] * dr - summed[:, :, 1] * di
    turned_i = summed[:, :, 0] * di + summed[:, :, 1] * dr
    turned = jnp.stack([turned_r, turned_i], axis=2)
    col_groups = jnp.arange(CROP // PHASES, dtype=jnp.int32)
    gr, gi = _cos_sin(jnp.mod(offsets[:, None] * col_groups[None, :], BLOCK), BLOCK)
    col_op = jnp.stack([gr, -gi], axis=0)
    return jnp.einsum(
        "cvj,ltcv->jlt", col_op, turned, precision=lax.Precision.HIGH, preferred_element_type=jnp.float32
    ) * (1.0 / GRID)


def body(voltages, model_vis, kernel_u, kernel_v, pair_slot, slot_block, slot_count):
    local_antennas = voltages.shape[1]
    direct = voltages.reshape(voltages.shape[0], 1, local_antennas, 2 * SAMPLES)
    turned = lax.all_to_all(direct, ("grp", "chan"), split_axis=0, concat_axis=1, tiled=True)
    antenna_volts = turned.reshape(ANTENNAS, 2 * SAMPLES)
    slot_grids = grid_slots(
        antenna_volts, model_vis[0], kernel_u[0], kernel_v[0], pair_slot[0], slot_count
    )
    image_t = channel_image(slot_grids, slot_block[0])
    n_chan = lax.axis_size("chan")
    n_grp = lax.axis_size("grp")
    rows_per = ROWS // n_chan
    groups_per = CROP // PHASES // n_grp
    send = image_t.reshape(n_grp, groups_per, n_chan, rows_per * PHASES).transpose(0, 2, 1, 3)
    send = send.reshape(n_grp * n_chan, groups_per, rows_per * PHASES).astype(jnp.bfloat16)
    got = lax.all_to_all(send, ("grp", "chan"), split_axis=0, concat_axis=0, tiled=True)
    summed = got.astype(jnp.float32).sum(axis=0).reshape(groups_per, rows_per, PHASES)
    return summed.transpose(1, 0, 2).reshape(rows_per, groups_per * PHASES)


def solution(mesh):
    in_specs = (
        P(None, ("grp", "chan"), None),
        P(("grp", "chan"), None, None, None, None),
        P(("grp", "chan"), None, None, None),
        P(("grp", "chan"), None, None, None),
        P(("grp", "chan"), None),
        P(("grp", "chan"), None),
        P(("grp", "chan")),
    )
    out_specs = P("chan", "grp")
    return jax.shard_map(body, mesh=mesh, in_specs=in_specs, out_specs=out_specs, check_vma=False)
```

```python
import math

import jax
import jax.numpy as jnp
import numpy as np
from jax import lax
from jax.experimental import pallas as pl
from jax.experimental.pallas import tpu as pltpu
from jax.sharding import PartitionSpec as P

ANTENNAS = 2048
SAMPLES = 64
TILE = 128
BLOCK = 128
GRID = 4096
CROP = 2048
SLOTS = 16
ROWS = 256
TILES = 16
PAIRS = 136
PHASES = 32

TWO_PI = 2.0 * math.pi


def _grid_kernel(ptab, qtab, slot_ref, count_ref, v_ref, w_ref, model_ref, ku_ref, kvt_ref, out_ref, acc_ref):
    acc_ref[...] = jnp.zeros_like(acc_ref)
    count = count_ref[0]

    def body(k, carry):
        p = ptab[k]
        q = qtab[k]
        slot = slot_ref[k]
        gram = jnp.dot(v_ref[p], w_ref[q], preferred_element_type=jnp.float32)
        model = jnp.concatenate([model_ref[k, 0], model_ref[k, 1]], axis=1).astype(jnp.float32)
        residual = (gram * (1.0 / SAMPLES) - model).astype(jnp.bfloat16)
        half = jnp.dot(ku_ref[p], residual, preferred_element_type=jnp.float32).astype(jnp.bfloat16)
        half_rows = jnp.concatenate([half[:, :TILE], half[:, TILE:]], axis=0)
        tile = jnp.dot(half_rows, kvt_ref[q], preferred_element_type=jnp.float32)
        live = (slot < count) & (slot >= 0)
        slot_c = jnp.clip(slot, 0, SLOTS - 1)

        acc_ref[slot_c] += jnp.where(live, tile, 0.0)
        return carry

    lax.fori_loop(0, PAIRS, body, 0, unroll=8)
    out_ref[...] = acc_ref[...].astype(out_ref.dtype)


def grid_slots(antenna_volts, model_one, kernel_u_one, kernel_v_one, slots_one, count_one):
    row_tiles, col_tiles = np.triu_indices(TILES)
    ptab = jnp.asarray(row_tiles, jnp.int32)
    qtab = jnp.asarray(col_tiles, jnp.int32)
    swapped = jnp.concatenate([-antenna_volts[:, SAMPLES:], antenna_volts[:, :SAMPLES]], axis=1)
    tiles = antenna_volts.reshape(TILES, TILE, 2 * SAMPLES)
    turned = jnp.concatenate(
        [tiles.transpose(0, 2, 1), swapped.reshape(TILES, TILE, 2 * SAMPLES).transpose(0, 2, 1)], axis=2
    )
    kv_turned = kernel_v_one.transpose(0, 2, 1)
    smem = pl.BlockSpec(memory_space=pltpu.SMEM)
    vmem = pl.BlockSpec(memory_space=pltpu.VMEM)
    flops = PAIRS * 3 * 2 * (2 * TILE) * TILE * TILE
    return pl.pallas_call(
        _grid_kernel,
        out_shape=jax.ShapeDtypeStruct((SLOTS, 2 * BLOCK, BLOCK), jnp.bfloat16),
        in_specs=[smem, smem, smem, smem, vmem, vmem, vmem, vmem, vmem],
        out_specs=vmem,
        scratch_shapes=[pltpu.VMEM((SLOTS, 2 * BLOCK, BLOCK), jnp.float32)],
        compiler_params=pltpu.CompilerParams(vmem_limit_bytes=48 * 1024 * 1024),
        cost_estimate=pl.CostEstimate(flops=flops, transcendentals=0, bytes_accessed=11 * 1024 * 1024),
    )(ptab, qtab, slots_one, count_one, tiles, turned, model_one, kernel_u_one, kv_turned)


def _cos_sin(index, period):
    angles = index.astype(jnp.float32) * (TWO_PI / period)
    return jnp.cos(angles), jnp.sin(angles)


def channel_image(slot_grids, blocks_here):
    per_side = GRID // BLOCK
    grids = slot_grids.reshape(SLOTS, 2, BLOCK, BLOCK).astype(jnp.float32)
    block_rows = blocks_here // per_side
    block_cols = blocks_here % per_side
    offsets = jnp.arange(BLOCK, dtype=jnp.int32)
    pixel_rows = jnp.arange(ROWS, dtype=jnp.int32) - ROWS // 2
    er, ei = _cos_sin(jnp.mod(block_rows[:, None] * pixel_rows[None, :], PHASES), PHASES)
    br0, bi0 = _cos_sin(jnp.mod(pixel_rows[:, None] * (offsets - GRID // 2)[None, :], GRID), GRID)
    ar = er[:, :, None] * br0[None] - ei[:, :, None] * bi0[None]
    ai = er[:, :, None] * bi0[None] + ei[:, :, None] * br0[None]
    row_op = jnp.stack([jnp.stack([ar, -ai], axis=2), jnp.stack([ai, ar], axis=2)], axis=1)
    rows_done = jnp.einsum(
        "sclku,skuv->sclv", row_op, grids, precision=lax.Precision.HIGH, preferred_element_type=jnp.float32
    )
    phases = jnp.arange(PHASES, dtype=jnp.int32)
    zr, zi = _cos_sin(jnp.mod(phases[:, None] * block_cols[None, :], PHASES), PHASES)
    phase_op = jnp.stack([jnp.stack([zr, -zi], axis=2), jnp.stack([zi, zr], axis=2)], axis=1)
    summed = jnp.einsum(
        "tcsk,sklv->ltcv", phase_op, rows_done, precision=lax.Precision.HIGH, preferred_element_type=jnp.float32
    )
    dr, di = _cos_sin(jnp.mod((phases[:, None] - GRID // 4) * offsets[None, :] - (GRID // 2) * phases[:, None], GRID), GRID)
    turned_r = summed[:, :, 0] * dr - summed[:, :, 1] * di
    turned_i = summed[:, :, 0] * di + summed[:, :, 1] * dr
    turned = jnp.stack([turned_r, turned_i], axis=2)
    col_groups = jnp.arange(CROP // PHASES, dtype=jnp.int32)
    gr, gi = _cos_sin(jnp.mod(offsets[:, None] * col_groups[None, :], BLOCK), BLOCK)
    col_op = jnp.stack([gr, -gi], axis=0)
    image = lax.dot_general(
        col_op.reshape(2 * BLOCK, CROP // PHASES),
        turned.reshape(ROWS * PHASES, 2 * BLOCK),
        (((0,), (1,)), ((), ())),
        precision=lax.Precision.HIGH,
        preferred_element_type=jnp.float32,
    )
    return (image * (1.0 / GRID)).reshape(CROP // PHASES, ROWS, PHASES)


def body(voltages, model_vis, kernel_u, kernel_v, pair_slot, slot_block, slot_count):
    local_antennas = voltages.shape[1]
    direct = voltages.reshape(voltages.shape[0], 1, local_antennas, 2 * SAMPLES)
    turned = lax.all_to_all(direct, ("grp", "chan"), split_axis=0, concat_axis=1, tiled=True)
    antenna_volts = turned.reshape(ANTENNAS, 2 * SAMPLES)
    slot_grids = grid_slots(
        antenna_volts, model_vis[0], kernel_u[0], kernel_v[0], pair_slot[0], slot_count
    )
    image_t = channel_image(slot_grids, slot_block[0])
    n_chan = lax.axis_size("chan")
    n_grp = lax.axis_size("grp")
    rows_per = ROWS // n_chan
    groups_per = CROP // PHASES // n_grp
    send = image_t.reshape(n_grp, groups_per, n_chan, rows_per * PHASES).transpose(0, 2, 1, 3)
    send = send.reshape(n_grp * n_chan, groups_per, rows_per * PHASES).astype(jnp.bfloat16)
    got = lax.all_to_all(send, ("grp", "chan"), split_axis=0, concat_axis=0, tiled=True)
    summed = got.astype(jnp.float32).sum(axis=0).reshape(groups_per, rows_per, PHASES)
    return summed.transpose(1, 0, 2).reshape(rows_per, groups_per * PHASES)


def solution(mesh):
    in_specs = (
        P(None, ("grp", "chan"), None),
        P(("grp", "chan"), None, None, None, None),
        P(("grp", "chan"), None, None, None),
        P(("grp", "chan"), None, None, None),
        P(("grp", "chan"), None),
        P(("grp", "chan"), None),
        P(("grp", "chan")),
    )
    out_specs = P("chan", "grp")
    return jax.shard_map(body, mesh=mesh, in_specs=in_specs, out_specs=out_specs, check_vma=False)
```

```python
import math

import jax
import jax.numpy as jnp
import numpy as np
from jax import lax
from jax.experimental import pallas as pl
from jax.experimental.pallas import tpu as pltpu
from jax.sharding import PartitionSpec as P

ANTENNAS = 2048
SAMPLES = 64
TILE = 128
BLOCK = 128
GRID = 4096
CROP = 2048
SLOTS = 16
ROWS = 256
TILES = 16
PAIRS = 136
PHASES = 32

TWO_PI = 2.0 * math.pi


def _grid_kernel(ptab, qtab, slot_ref, count_ref, v_ref, w_ref, model_ref, ku_ref, kvt_ref, out_ref, acc_ref):
    acc_ref[...] = jnp.zeros_like(acc_ref)
    count = count_ref[0]

    def body(k, carry):
        p = ptab[k]
        q = qtab[k]
        slot = slot_ref[k]
        gram = jnp.dot(v_ref[p], w_ref[q], preferred_element_type=jnp.float32)
        model = jnp.concatenate([model_ref[k, 0], model_ref[k, 1]], axis=1).astype(jnp.float32)
        residual = (gram * (1.0 / SAMPLES) - model).astype(jnp.bfloat16)
        half = jnp.dot(ku_ref[p], residual, preferred_element_type=jnp.float32).astype(jnp.bfloat16)
        half_rows = jnp.concatenate([half[:, :TILE], half[:, TILE:]], axis=0)
        tile = jnp.dot(half_rows, kvt_ref[q], preferred_element_type=jnp.float32)
        live = (slot < count) & (slot >= 0)
        slot_c = jnp.clip(slot, 0, SLOTS - 1)

        acc_ref[slot_c] += jnp.where(live, tile, 0.0)
        return carry

    lax.fori_loop(0, PAIRS, body, 0, unroll=17)
    out_ref[...] = acc_ref[...].astype(out_ref.dtype)


def grid_slots(antenna_volts, model_one, kernel_u_one, kernel_v_one, slots_one, count_one):
    row_tiles, col_tiles = np.triu_indices(TILES)
    ptab = jnp.asarray(row_tiles, jnp.int32)
    qtab = jnp.asarray(col_tiles, jnp.int32)
    swapped = jnp.concatenate([-antenna_volts[:, SAMPLES:], antenna_volts[:, :SAMPLES]], axis=1)
    tiles = antenna_volts.reshape(TILES, TILE, 2 * SAMPLES)
    turned = jnp.concatenate(
        [tiles.transpose(0, 2, 1), swapped.reshape(TILES, TILE, 2 * SAMPLES).transpose(0, 2, 1)], axis=2
    )
    kv_turned = kernel_v_one.transpose(0, 2, 1)
    smem = pl.BlockSpec(memory_space=pltpu.SMEM)
    vmem = pl.BlockSpec(memory_space=pltpu.VMEM)
    flops = PAIRS * 3 * 2 * (2 * TILE) * TILE * TILE
    return pl.pallas_call(
        _grid_kernel,
        out_shape=jax.ShapeDtypeStruct((SLOTS, 2 * BLOCK, BLOCK), jnp.bfloat16),
        in_specs=[smem, smem, smem, smem, vmem, vmem, vmem, vmem, vmem],
        out_specs=vmem,
        scratch_shapes=[pltpu.VMEM((SLOTS, 2 * BLOCK, BLOCK), jnp.float32)],
        compiler_params=pltpu.CompilerParams(vmem_limit_bytes=48 * 1024 * 1024),
        cost_estimate=pl.CostEstimate(flops=flops, transcendentals=0, bytes_accessed=11 * 1024 * 1024),
    )(ptab, qtab, slots_one, count_one, tiles, turned, model_one, kernel_u_one, kv_turned)


def _cos_sin(index, period):
    angles = index.astype(jnp.float32) * (TWO_PI / period)
    return jnp.cos(angles), jnp.sin(angles)


def channel_image(slot_grids, blocks_here):
    per_side = GRID // BLOCK
    grids = slot_grids.reshape(SLOTS, 2, BLOCK, BLOCK).astype(jnp.float32)
    block_rows = blocks_here // per_side
    block_cols = blocks_here % per_side
    offsets = jnp.arange(BLOCK, dtype=jnp.int32)
    pixel_rows = jnp.arange(ROWS, dtype=jnp.int32) - ROWS // 2
    er, ei = _cos_sin(jnp.mod(block_rows[:, None] * pixel_rows[None, :], PHASES), PHASES)
    br0, bi0 = _cos_sin(jnp.mod(pixel_rows[:, None] * (offsets - GRID // 2)[None, :], GRID), GRID)
    ar = er[:, :, None] * br0[None] - ei[:, :, None] * bi0[None]
    ai = er[:, :, None] * bi0[None] + ei[:, :, None] * br0[None]
    row_op = jnp.stack([jnp.stack([ar, -ai], axis=2), jnp.stack([ai, ar], axis=2)], axis=1)
    rows_done = jnp.einsum(
        "sclku,skuv->sclv", row_op, grids, precision=lax.Precision.HIGH, preferred_element_type=jnp.float32
    )
    phases = jnp.arange(PHASES, dtype=jnp.int32)
    zr, zi = _cos_sin(jnp.mod(phases[:, None] * block_cols[None, :], PHASES), PHASES)
    phase_op = jnp.stack([jnp.stack([zr, -zi], axis=2), jnp.stack([zi, zr], axis=2)], axis=1)
    summed = jnp.einsum(
        "tcsk,sklv->ltcv", phase_op, rows_done, precision=lax.Precision.HIGH, preferred_element_type=jnp.float32
    )
    dr, di = _cos_sin(jnp.mod((phases[:, None] - GRID // 4) * offsets[None, :] - (GRID // 2) * phases[:, None], GRID), GRID)
    turned_r = summed[:, :, 0] * dr - summed[:, :, 1] * di
    turned_i = summed[:, :, 0] * di + summed[:, :, 1] * dr
    turned = jnp.concatenate([turned_r, turned_i], axis=2)
    col_groups = jnp.arange(CROP // PHASES, dtype=jnp.int32)
    gr, gi = _cos_sin(jnp.mod(offsets[:, None] * col_groups[None, :], BLOCK), BLOCK)
    col_op = jnp.concatenate([gr, -gi], axis=0)
    image = lax.dot_general(
        col_op,
        turned.reshape(ROWS * PHASES, 2 * BLOCK),
        (((0,), (1,)), ((), ())),
        precision=lax.Precision.HIGH,
        preferred_element_type=jnp.float32,
    )
    return (image * (1.0 / GRID)).reshape(CROP // PHASES, ROWS, PHASES)


def body(voltages, model_vis, kernel_u, kernel_v, pair_slot, slot_block, slot_count):
    local_antennas = voltages.shape[1]
    direct = voltages.reshape(voltages.shape[0], 1, local_antennas, 2 * SAMPLES)
    turned = lax.all_to_all(direct, ("grp", "chan"), split_axis=0, concat_axis=1, tiled=True)
    antenna_volts = turned.reshape(ANTENNAS, 2 * SAMPLES)
    slot_grids = grid_slots(
        antenna_volts, model_vis[0], kernel_u[0], kernel_v[0], pair_slot[0], slot_count
    )
    image_t = channel_image(slot_grids, slot_block[0])
    n_chan = lax.axis_size("chan")
    n_grp = lax.axis_size("grp")
    rows_per = ROWS // n_chan
    groups_per = CROP // PHASES // n_grp
    send = image_t.reshape(n_grp, groups_per, n_chan, rows_per * PHASES).transpose(0, 2, 1, 3)
    send = send.reshape(n_grp * n_chan, groups_per, rows_per * PHASES).astype(jnp.bfloat16)
    got = lax.all_to_all(send, ("grp", "chan"), split_axis=0, concat_axis=0, tiled=True)
    summed = got.astype(jnp.float32).sum(axis=0).reshape(groups_per, rows_per, PHASES)
    return summed.transpose(1, 0, 2).reshape(rows_per, groups_per * PHASES)


def solution(mesh):
    in_specs = (
        P(None, ("grp", "chan"), None),
        P(("grp", "chan"), None, None, None, None),
        P(("grp", "chan"), None, None, None),
        P(("grp", "chan"), None, None, None),
        P(("grp", "chan"), None),
        P(("grp", "chan"), None),
        P(("grp", "chan")),
    )
    out_specs = P("chan", "grp")
    return jax.shard_map(body, mesh=mesh, in_specs=in_specs, out_specs=out_specs, check_vma=False)
```

```python
import math

import jax
import jax.numpy as jnp
import numpy as np
from jax import lax
from jax.experimental import pallas as pl
from jax.experimental.pallas import tpu as pltpu
from jax.sharding import PartitionSpec as P

ANTENNAS = 2048
SAMPLES = 64
TILE = 128
BLOCK = 128
GRID = 4096
CROP = 2048
SLOTS = 16
ROWS = 256
TILES = 16
PAIRS = 136
PHASES = 32

TWO_PI = 2.0 * math.pi


PAIRS_PER_STEP = 8


def _grid_kernel(ptab, qtab, slot_ref, count_ref, v_ref, w_ref, model_ref, ku_ref, kvt_ref, out_ref, acc_ref):
    step = pl.program_id(0)

    @pl.when(step == 0)
    def _():
        acc_ref[...] = jnp.zeros_like(acc_ref)

    count = count_ref[0]

    def body(i, carry):
        k = step * PAIRS_PER_STEP + i
        p = ptab[k]
        q = qtab[k]
        slot = slot_ref[k]
        gram = jnp.dot(v_ref[p], w_ref[q], preferred_element_type=jnp.float32)
        model = jnp.concatenate([model_ref[i, 0], model_ref[i, 1]], axis=1).astype(jnp.float32)
        residual = (gram * (1.0 / SAMPLES) - model).astype(jnp.bfloat16)
        half = jnp.dot(ku_ref[p], residual, preferred_element_type=jnp.float32).astype(jnp.bfloat16)
        half_rows = jnp.concatenate([half[:, :TILE], half[:, TILE:]], axis=0)
        tile = jnp.dot(half_rows, kvt_ref[q], preferred_element_type=jnp.float32)
        live = (slot < count) & (slot >= 0)
        slot_c = jnp.clip(slot, 0, SLOTS - 1)
        acc_ref[slot_c] += jnp.where(live, tile, 0.0)
        return carry

    lax.fori_loop(0, PAIRS_PER_STEP, body, 0, unroll=True)

    @pl.when(step == pl.num_programs(0) - 1)
    def _():
        out_ref[...] = acc_ref[...].astype(out_ref.dtype)


def grid_slots(antenna_volts, model_one, kernel_u_one, kernel_v_one, slots_one, count_one):
    row_tiles, col_tiles = np.triu_indices(TILES)
    ptab = jnp.asarray(row_tiles, jnp.int32)
    qtab = jnp.asarray(col_tiles, jnp.int32)
    swapped = jnp.concatenate([-antenna_volts[:, SAMPLES:], antenna_volts[:, :SAMPLES]], axis=1)
    tiles = antenna_volts.reshape(TILES, TILE, 2 * SAMPLES)
    turned = jnp.concatenate(
        [tiles.transpose(0, 2, 1), swapped.reshape(TILES, TILE, 2 * SAMPLES).transpose(0, 2, 1)], axis=2
    )
    kv_turned = kernel_v_one.transpose(0, 2, 1)
    steps = PAIRS // PAIRS_PER_STEP

    def whole(shape):
        return pl.BlockSpec(shape, lambda s, *_: (0,) * len(shape))

    flops = PAIRS * 3 * 2 * (2 * TILE) * TILE * TILE
    grid_spec = pltpu.PrefetchScalarGridSpec(
        num_scalar_prefetch=4,
        grid=(steps,),
        in_specs=[
            whole((TILES, TILE, 2 * SAMPLES)),
            whole((TILES, 2 * SAMPLES, 2 * TILE)),
            pl.BlockSpec((PAIRS_PER_STEP, 2, TILE, TILE), lambda s, *_: (s, 0, 0, 0)),
            whole((TILES, BLOCK, TILE)),
            whole((TILES, TILE, BLOCK)),
        ],
        out_specs=whole((SLOTS, 2 * BLOCK, BLOCK)),
        scratch_shapes=[pltpu.VMEM((SLOTS, 2 * BLOCK, BLOCK), jnp.float32)],
    )
    return pl.pallas_call(
        _grid_kernel,
        out_shape=jax.ShapeDtypeStruct((SLOTS, 2 * BLOCK, BLOCK), jnp.bfloat16),
        grid_spec=grid_spec,
        compiler_params=pltpu.CompilerParams(
            dimension_semantics=("arbitrary",), vmem_limit_bytes=48 * 1024 * 1024
        ),
        cost_estimate=pl.CostEstimate(flops=flops, transcendentals=0, bytes_accessed=11 * 1024 * 1024),
    )(ptab, qtab, slots_one, count_one, tiles, turned, model_one, kernel_u_one, kv_turned)


def _cos_sin(index, period):
    angles = index.astype(jnp.float32) * (TWO_PI / period)
    return jnp.cos(angles), jnp.sin(angles)


def channel_image(slot_grids, blocks_here):
    per_side = GRID // BLOCK
    grids = slot_grids.reshape(SLOTS, 2, BLOCK, BLOCK).astype(jnp.float32)
    block_rows = blocks_here // per_side
    block_cols = blocks_here % per_side
    offsets = jnp.arange(BLOCK, dtype=jnp.int32)
    pixel_rows = jnp.arange(ROWS, dtype=jnp.int32) - ROWS // 2
    er, ei = _cos_sin(jnp.mod(block_rows[:, None] * pixel_rows[None, :], PHASES), PHASES)
    br0, bi0 = _cos_sin(jnp.mod(pixel_rows[:, None] * (offsets - GRID // 2)[None, :], GRID), GRID)
    ar = er[:, :, None] * br0[None] - ei[:, :, None] * bi0[None]
    ai = er[:, :, None] * bi0[None] + ei[:, :, None] * br0[None]
    row_op = jnp.stack([jnp.stack([ar, -ai], axis=2), jnp.stack([ai, ar], axis=2)], axis=1)
    rows_done = jnp.einsum(
        "sclku,skuv->sclv", row_op, grids, precision=lax.Precision.HIGH, preferred_element_type=jnp.float32
    )
    phases = jnp.arange(PHASES, dtype=jnp.int32)
    zr, zi = _cos_sin(jnp.mod(phases[:, None] * block_cols[None, :], PHASES), PHASES)
    phase_op = jnp.stack([jnp.stack([zr, -zi], axis=2), jnp.stack([zi, zr], axis=2)], axis=1)
    summed = jnp.einsum(
        "tcsk,sklv->ltcv", phase_op, rows_done, precision=lax.Precision.HIGH, preferred_element_type=jnp.float32
    )
    dr, di = _cos_sin(jnp.mod((phases[:, None] - GRID // 4) * offsets[None, :] - (GRID // 2) * phases[:, None], GRID), GRID)
    turned_r = summed[:, :, 0] * dr - summed[:, :, 1] * di
    turned_i = summed[:, :, 0] * di + summed[:, :, 1] * dr
    turned = jnp.concatenate([turned_r, turned_i], axis=2)
    col_groups = jnp.arange(CROP // PHASES, dtype=jnp.int32)
    gr, gi = _cos_sin(jnp.mod(offsets[:, None] * col_groups[None, :], BLOCK), BLOCK)
    col_op = jnp.concatenate([gr, -gi], axis=0)
    image = lax.dot_general(
        col_op,
        turned.reshape(ROWS * PHASES, 2 * BLOCK),
        (((0,), (1,)), ((), ())),
        precision=lax.Precision.HIGH,
        preferred_element_type=jnp.float32,
    )
    return (image * (1.0 / GRID)).reshape(CROP // PHASES, ROWS, PHASES)


def body(voltages, model_vis, kernel_u, kernel_v, pair_slot, slot_block, slot_count):
    local_antennas = voltages.shape[1]
    direct = voltages.reshape(voltages.shape[0], 1, local_antennas, 2 * SAMPLES)
    turned = lax.all_to_all(direct, ("grp", "chan"), split_axis=0, concat_axis=1, tiled=True)
    antenna_volts = turned.reshape(ANTENNAS, 2 * SAMPLES)
    slot_grids = grid_slots(
        antenna_volts, model_vis[0], kernel_u[0], kernel_v[0], pair_slot[0], slot_count
    )
    image_t = channel_image(slot_grids, slot_block[0])
    n_chan = lax.axis_size("chan")
    n_grp = lax.axis_size("grp")
    rows_per = ROWS // n_chan
    groups_per = CROP // PHASES // n_grp
    send = image_t.reshape(n_grp, groups_per, n_chan, rows_per * PHASES).transpose(0, 2, 1, 3)
    send = send.reshape(n_grp * n_chan, groups_per, rows_per * PHASES).astype(jnp.bfloat16)
    got = lax.all_to_all(send, ("grp", "chan"), split_axis=0, concat_axis=0, tiled=True)
    summed = got.astype(jnp.float32).sum(axis=0).reshape(groups_per, rows_per, PHASES)
    return summed.transpose(1, 0, 2).reshape(rows_per, groups_per * PHASES)


def solution(mesh):
    in_specs = (
        P(None, ("grp", "chan"), None),
        P(("grp", "chan"), None, None, None, None),
        P(("grp", "chan"), None, None, None),
        P(("grp", "chan"), None, None, None),
        P(("grp", "chan"), None),
        P(("grp", "chan"), None),
        P(("grp", "chan")),
    )
    out_specs = P("chan", "grp")
    return jax.shard_map(body, mesh=mesh, in_specs=in_specs, out_specs=out_specs, check_vma=False)
```

```python
import math

import jax
import jax.numpy as jnp
import numpy as np
from jax import lax
from jax.experimental import pallas as pl
from jax.experimental.pallas import tpu as pltpu
from jax.sharding import PartitionSpec as P

ANTENNAS = 2048
SAMPLES = 64
TILE = 128
BLOCK = 128
GRID = 4096
CROP = 2048
SLOTS = 16
ROWS = 256
TILES = 16
PAIRS = 136
PHASES = 32

TWO_PI = 2.0 * math.pi


def _grid_kernel(ptab, qtab, slot_ref, count_ref, v_ref, w_ref, model_ref, ku_ref, kvt_ref, out_ref, acc_ref):
    acc_ref[...] = jnp.zeros_like(acc_ref)
    count = count_ref[0]

    def body(k, carry):
        p = ptab[k]
        q = qtab[k]
        slot = slot_ref[k]
        gram = jnp.dot(v_ref[p], w_ref[q], preferred_element_type=jnp.float32)
        model = jnp.concatenate([model_ref[k, 0], model_ref[k, 1]], axis=1).astype(jnp.float32)
        residual = (gram * (1.0 / SAMPLES) - model).astype(jnp.bfloat16)
        half = jnp.dot(ku_ref[p], residual, preferred_element_type=jnp.float32).astype(jnp.bfloat16)
        half_rows = jnp.concatenate([half[:, :TILE], half[:, TILE:]], axis=0)
        tile = jnp.dot(half_rows, kvt_ref[q], preferred_element_type=jnp.float32)
        live = (slot < count) & (slot >= 0)
        slot_c = jnp.clip(slot, 0, SLOTS - 1)

        acc_ref[slot_c] += jnp.where(live, tile, 0.0)
        return carry

    lax.fori_loop(0, PAIRS, body, 0, unroll=34)
    out_ref[...] = acc_ref[...].astype(out_ref.dtype)


def grid_slots(antenna_volts, model_one, kernel_u_one, kernel_v_one, slots_one, count_one):
    row_tiles, col_tiles = np.triu_indices(TILES)
    ptab = jnp.asarray(row_tiles, jnp.int32)
    qtab = jnp.asarray(col_tiles, jnp.int32)
    swapped = jnp.concatenate([-antenna_volts[:, SAMPLES:], antenna_volts[:, :SAMPLES]], axis=1)
    tiles = antenna_volts.reshape(TILES, TILE, 2 * SAMPLES)
    turned = jnp.concatenate(
        [tiles.transpose(0, 2, 1), swapped.reshape(TILES, TILE, 2 * SAMPLES).transpose(0, 2, 1)], axis=2
    )
    kv_turned = kernel_v_one.transpose(0, 2, 1)
    smem = pl.BlockSpec(memory_space=pltpu.SMEM)
    vmem = pl.BlockSpec(memory_space=pltpu.VMEM)
    flops = PAIRS * 3 * 2 * (2 * TILE) * TILE * TILE
    return pl.pallas_call(
        _grid_kernel,
        out_shape=jax.ShapeDtypeStruct((SLOTS, 2 * BLOCK, BLOCK), jnp.bfloat16),
        in_specs=[smem, smem, smem, smem, vmem, vmem, vmem, vmem, vmem],
        out_specs=vmem,
        scratch_shapes=[pltpu.VMEM((SLOTS, 2 * BLOCK, BLOCK), jnp.float32)],
        compiler_params=pltpu.CompilerParams(vmem_limit_bytes=48 * 1024 * 1024),
        cost_estimate=pl.CostEstimate(flops=flops, transcendentals=0, bytes_accessed=11 * 1024 * 1024),
    )(ptab, qtab, slots_one, count_one, tiles, turned, model_one, kernel_u_one, kv_turned)


def _cos_sin(index, period):
    angles = index.astype(jnp.float32) * (TWO_PI / period)
    return jnp.cos(angles), jnp.sin(angles)


def channel_image(slot_grids, blocks_here):
    per_side = GRID // BLOCK
    grids = slot_grids.reshape(SLOTS, 2, BLOCK, BLOCK).astype(jnp.float32)
    block_rows = blocks_here // per_side
    block_cols = blocks_here % per_side
    offsets = jnp.arange(BLOCK, dtype=jnp.int32)
    pixel_rows = jnp.arange(ROWS, dtype=jnp.int32) - ROWS // 2
    er, ei = _cos_sin(jnp.mod(block_rows[:, None] * pixel_rows[None, :], PHASES), PHASES)
    br0, bi0 = _cos_sin(jnp.mod(pixel_rows[:, None] * (offsets - GRID // 2)[None, :], GRID), GRID)
    ar = er[:, :, None] * br0[None] - ei[:, :, None] * bi0[None]
    ai = er[:, :, None] * bi0[None] + ei[:, :, None] * br0[None]
    row_op = jnp.stack([jnp.stack([ar, -ai], axis=2), jnp.stack([ai, ar], axis=2)], axis=1)
    rows_done = jnp.einsum(
        "sclku,skuv->sclv", row_op, grids, precision=lax.Precision.HIGH, preferred_element_type=jnp.float32
    )
    phases = jnp.arange(PHASES, dtype=jnp.int32)
    zr, zi = _cos_sin(jnp.mod(phases[:, None] * block_cols[None, :], PHASES), PHASES)
    phase_op = jnp.stack([jnp.stack([zr, -zi], axis=2), jnp.stack([zi, zr], axis=2)], axis=1)
    summed = jnp.einsum(
        "tcsk,sklv->ltcv", phase_op, rows_done, precision=lax.Precision.HIGH, preferred_element_type=jnp.float32
    )
    dr, di = _cos_sin(jnp.mod((phases[:, None] - GRID // 4) * offsets[None, :] - (GRID // 2) * phases[:, None], GRID), GRID)
    turned_r = summed[:, :, 0] * dr - summed[:, :, 1] * di
    turned_i = summed[:, :, 0] * di + summed[:, :, 1] * dr
    turned = jnp.concatenate([turned_r, turned_i], axis=2)
    col_groups = jnp.arange(CROP // PHASES, dtype=jnp.int32)
    gr, gi = _cos_sin(jnp.mod(offsets[:, None] * col_groups[None, :], BLOCK), BLOCK)
    col_op = jnp.concatenate([gr, -gi], axis=0)
    image = lax.dot_general(
        col_op,
        turned.reshape(ROWS * PHASES, 2 * BLOCK),
        (((0,), (1,)), ((), ())),
        precision=lax.Precision.HIGH,
        preferred_element_type=jnp.float32,
    )
    return (image * (1.0 / GRID)).reshape(CROP // PHASES, ROWS, PHASES)


def body(voltages, model_vis, kernel_u, kernel_v, pair_slot, slot_block, slot_count):
    local_antennas = voltages.shape[1]
    direct = voltages.reshape(voltages.shape[0], 1, local_antennas, 2 * SAMPLES)
    turned = lax.all_to_all(direct, ("grp", "chan"), split_axis=0, concat_axis=1, tiled=True)
    antenna_volts = turned.reshape(ANTENNAS, 2 * SAMPLES)
    slot_grids = grid_slots(
        antenna_volts, model_vis[0], kernel_u[0], kernel_v[0], pair_slot[0], slot_count
    )
    image_t = channel_image(slot_grids, slot_block[0])
    n_chan = lax.axis_size("chan")
    n_grp = lax.axis_size("grp")
    rows_per = ROWS // n_chan
    groups_per = CROP // PHASES // n_grp
    send = image_t.reshape(n_grp, groups_per, n_chan, rows_per * PHASES).transpose(0, 2, 1, 3)
    send = send.reshape(n_grp * n_chan, groups_per, rows_per * PHASES).astype(jnp.bfloat16)
    got = lax.all_to_all(send, ("grp", "chan"), split_axis=0, concat_axis=0, tiled=True)
    summed = got.astype(jnp.float32).sum(axis=0).reshape(groups_per, rows_per, PHASES)
    return summed.transpose(1, 0, 2).reshape(rows_per, groups_per * PHASES)


def solution(mesh):
    in_specs = (
        P(None, ("grp", "chan"), None),
        P(("grp", "chan"), None, None, None, None),
        P(("grp", "chan"), None, None, None),
        P(("grp", "chan"), None, None, None),
        P(("grp", "chan"), None),
        P(("grp", "chan"), None),
        P(("grp", "chan")),
    )
    out_specs = P("chan", "grp")
    return jax.shard_map(body, mesh=mesh, in_specs=in_specs, out_specs=out_specs, check_vma=False)
```

```python
import math

import jax
import jax.numpy as jnp
import numpy as np
from jax import lax
from jax.experimental import pallas as pl
from jax.experimental.pallas import tpu as pltpu
from jax.sharding import PartitionSpec as P

ANTENNAS = 2048
SAMPLES = 64
TILE = 128
BLOCK = 128
GRID = 4096
CROP = 2048
SLOTS = 16
ROWS = 256
TILES = 16
PAIRS = 136
PHASES = 32

TWO_PI = 2.0 * math.pi


def _grid_kernel(ptab, qtab, slot_ref, count_ref, v_ref, w_ref, model_ref, ku_ref, kvt_ref, out_ref, acc_ref):
    acc_ref[...] = jnp.zeros_like(acc_ref)
    count = count_ref[0]

    def body(k, carry):
        p = ptab[k]
        q = qtab[k]
        slot = slot_ref[k]
        gram = jnp.dot(v_ref[p], w_ref[q], preferred_element_type=jnp.float32)
        model = jnp.concatenate([model_ref[k, 0], model_ref[k, 1]], axis=1).astype(jnp.float32)
        residual = (gram * (1.0 / SAMPLES) - model).astype(jnp.bfloat16)
        half = jnp.dot(ku_ref[p], residual, preferred_element_type=jnp.float32).astype(jnp.bfloat16)
        half_rows = jnp.concatenate([half[:, :TILE], half[:, TILE:]], axis=0)
        tile = jnp.dot(half_rows, kvt_ref[q], preferred_element_type=jnp.float32)
        live = (slot < count) & (slot >= 0)
        slot_c = jnp.clip(slot, 0, SLOTS - 1)

        acc_ref[slot_c] += jnp.where(live, tile, 0.0)
        return carry

    lax.fori_loop(0, PAIRS, body, 0, unroll=68)
    out_ref[...] = acc_ref[...].astype(out_ref.dtype)


def grid_slots(antenna_volts, model_one, kernel_u_one, kernel_v_one, slots_one, count_one):
    row_tiles, col_tiles = np.triu_indices(TILES)
    ptab = jnp.asarray(row_tiles, jnp.int32)
    qtab = jnp.asarray(col_tiles, jnp.int32)
    swapped = jnp.concatenate([-antenna_volts[:, SAMPLES:], antenna_volts[:, :SAMPLES]], axis=1)
    tiles = antenna_volts.reshape(TILES, TILE, 2 * SAMPLES)
    turned = jnp.concatenate(
        [tiles.transpose(0, 2, 1), swapped.reshape(TILES, TILE, 2 * SAMPLES).transpose(0, 2, 1)], axis=2
    )
    kv_turned = kernel_v_one.transpose(0, 2, 1)
    smem = pl.BlockSpec(memory_space=pltpu.SMEM)
    vmem = pl.BlockSpec(memory_space=pltpu.VMEM)
    flops = PAIRS * 3 * 2 * (2 * TILE) * TILE * TILE
    return pl.pallas_call(
        _grid_kernel,
        out_shape=jax.ShapeDtypeStruct((SLOTS, 2 * BLOCK, BLOCK), jnp.bfloat16),
        in_specs=[smem, smem, smem, smem, vmem, vmem, vmem, vmem, vmem],
        out_specs=vmem,
        scratch_shapes=[pltpu.VMEM((SLOTS, 2 * BLOCK, BLOCK), jnp.float32)],
        compiler_params=pltpu.CompilerParams(vmem_limit_bytes=48 * 1024 * 1024),
        cost_estimate=pl.CostEstimate(flops=flops, transcendentals=0, bytes_accessed=11 * 1024 * 1024),
    )(ptab, qtab, slots_one, count_one, tiles, turned, model_one, kernel_u_one, kv_turned)


def _cos_sin(index, period):
    angles = index.astype(jnp.float32) * (TWO_PI / period)
    return jnp.cos(angles), jnp.sin(angles)


def channel_image(slot_grids, blocks_here):
    per_side = GRID // BLOCK
    grids = slot_grids.reshape(SLOTS, 2, BLOCK, BLOCK).astype(jnp.float32)
    block_rows = blocks_here // per_side
    block_cols = blocks_here % per_side
    offsets = jnp.arange(BLOCK, dtype=jnp.int32)
    pixel_rows = jnp.arange(ROWS, dtype=jnp.int32) - ROWS // 2
    er, ei = _cos_sin(jnp.mod(block_rows[:, None] * pixel_rows[None, :], PHASES), PHASES)
    br0, bi0 = _cos_sin(jnp.mod(pixel_rows[:, None] * (offsets - GRID // 2)[None, :], GRID), GRID)
    ar = er[:, :, None] * br0[None] - ei[:, :, None] * bi0[None]
    ai = er[:, :, None] * bi0[None] + ei[:, :, None] * br0[None]
    row_op = jnp.stack([jnp.stack([ar, -ai], axis=2), jnp.stack([ai, ar], axis=2)], axis=1)
    rows_done = jnp.einsum(
        "sclku,skuv->sclv", row_op, grids, precision=lax.Precision.HIGH, preferred_element_type=jnp.float32
    )
    phases = jnp.arange(PHASES, dtype=jnp.int32)
    zr, zi = _cos_sin(jnp.mod(phases[:, None] * block_cols[None, :], PHASES), PHASES)
    phase_op = jnp.stack([jnp.stack([zr, -zi], axis=2), jnp.stack([zi, zr], axis=2)], axis=1)
    summed = jnp.einsum(
        "tcsk,sklv->ltcv", phase_op, rows_done, precision=lax.Precision.HIGH, preferred_element_type=jnp.float32
    )
    dr, di = _cos_sin(jnp.mod((phases[:, None] - GRID // 4) * offsets[None, :] - (GRID // 2) * phases[:, None], GRID), GRID)
    turned_r = summed[:, :, 0] * dr - summed[:, :, 1] * di
    turned_i = summed[:, :, 0] * di + summed[:, :, 1] * dr
    turned = jnp.concatenate([turned_r, turned_i], axis=2)
    col_groups = jnp.arange(CROP // PHASES, dtype=jnp.int32)
    gr, gi = _cos_sin(jnp.mod(offsets[:, None] * col_groups[None, :], BLOCK), BLOCK)
    col_op = jnp.concatenate([gr, -gi], axis=0)
    image = lax.dot_general(
        col_op,
        turned.reshape(ROWS * PHASES, 2 * BLOCK),
        (((0,), (1,)), ((), ())),
        precision=lax.Precision.HIGH,
        preferred_element_type=jnp.float32,
    )
    return (image * (1.0 / GRID)).reshape(CROP // PHASES, ROWS, PHASES)


def body(voltages, model_vis, kernel_u, kernel_v, pair_slot, slot_block, slot_count):
    local_antennas = voltages.shape[1]
    direct = voltages.reshape(voltages.shape[0], 1, local_antennas, 2 * SAMPLES)
    turned = lax.all_to_all(direct, ("grp", "chan"), split_axis=0, concat_axis=1, tiled=True)
    antenna_volts = turned.reshape(ANTENNAS, 2 * SAMPLES)
    slot_grids = grid_slots(
        antenna_volts, model_vis[0], kernel_u[0], kernel_v[0], pair_slot[0], slot_count
    )
    image_t = channel_image(slot_grids, slot_block[0])
    n_chan = lax.axis_size("chan")
    n_grp = lax.axis_size("grp")
    rows_per = ROWS // n_chan
    groups_per = CROP // PHASES // n_grp
    send = image_t.reshape(n_grp, groups_per, n_chan, rows_per * PHASES).transpose(0, 2, 1, 3)
    send = send.reshape(n_grp * n_chan, groups_per, rows_per * PHASES).astype(jnp.bfloat16)
    got = lax.all_to_all(send, ("grp", "chan"), split_axis=0, concat_axis=0, tiled=True)
    summed = got.astype(jnp.float32).sum(axis=0).reshape(groups_per, rows_per, PHASES)
    return summed.transpose(1, 0, 2).reshape(rows_per, groups_per * PHASES)


def solution(mesh):
    in_specs = (
        P(None, ("grp", "chan"), None),
        P(("grp", "chan"), None, None, None, None),
        P(("grp", "chan"), None, None, None),
        P(("grp", "chan"), None, None, None),
        P(("grp", "chan"), None),
        P(("grp", "chan"), None),
        P(("grp", "chan")),
    )
    out_specs = P("chan", "grp")
    return jax.shard_map(body, mesh=mesh, in_specs=in_specs, out_specs=out_specs, check_vma=False)
```

```python
import math

import jax
import jax.numpy as jnp
import numpy as np
from jax import lax
from jax.experimental import pallas as pl
from jax.experimental.pallas import tpu as pltpu
from jax.sharding import PartitionSpec as P

ANTENNAS = 2048
SAMPLES = 64
TILE = 128
BLOCK = 128
GRID = 4096
CROP = 2048
SLOTS = 16
ROWS = 256
TILES = 16
PAIRS = 136
PHASES = 32

TWO_PI = 2.0 * math.pi


def _grid_kernel(ptab, qtab, slot_ref, count_ref, v_ref, w_ref, model_ref, ku_ref, kvt_ref, out_ref, acc_ref):
    acc_ref[...] = jnp.zeros_like(acc_ref)
    count = count_ref[0]

    def body(k, carry):
        p = ptab[k]
        q = qtab[k]
        slot = slot_ref[k]
        gram = jnp.dot(v_ref[p], w_ref[q], preferred_element_type=jnp.float32)
        model = jnp.concatenate([model_ref[k, 0], model_ref[k, 1]], axis=1).astype(jnp.float32)
        residual = (gram * (1.0 / SAMPLES) - model).astype(jnp.bfloat16)
        half = jnp.dot(ku_ref[p], residual, preferred_element_type=jnp.float32).astype(jnp.bfloat16)
        half_rows = jnp.concatenate([half[:, :TILE], half[:, TILE:]], axis=0)
        tile = jnp.dot(half_rows, kvt_ref[q], preferred_element_type=jnp.float32)
        live = (slot < count) & (slot >= 0)
        slot_c = jnp.clip(slot, 0, SLOTS - 1)

        acc_ref[slot_c] += jnp.where(live, tile, 0.0)
        return carry

    lax.fori_loop(0, PAIRS, body, 0, unroll=68)
    out_ref[...] = acc_ref[...].astype(out_ref.dtype)


def grid_slots(antenna_volts, model_one, kernel_u_one, kernel_v_one, slots_one, count_one):
    row_tiles, col_tiles = np.triu_indices(TILES)
    ptab = jnp.asarray(row_tiles, jnp.int32)
    qtab = jnp.asarray(col_tiles, jnp.int32)
    swapped = jnp.concatenate([-antenna_volts[:, SAMPLES:], antenna_volts[:, :SAMPLES]], axis=1)
    tiles = antenna_volts.reshape(TILES, TILE, 2 * SAMPLES)
    turned = jnp.concatenate(
        [tiles.transpose(0, 2, 1), swapped.reshape(TILES, TILE, 2 * SAMPLES).transpose(0, 2, 1)], axis=2
    )
    kv_turned = kernel_v_one.transpose(0, 2, 1)
    smem = pl.BlockSpec(memory_space=pltpu.SMEM)
    vmem = pl.BlockSpec(memory_space=pltpu.VMEM)
    flops = PAIRS * 3 * 2 * (2 * TILE) * TILE * TILE
    return pl.pallas_call(
        _grid_kernel,
        out_shape=jax.ShapeDtypeStruct((SLOTS, 2 * BLOCK, BLOCK), jnp.bfloat16),
        in_specs=[smem, smem, smem, smem, vmem, vmem, vmem, vmem, vmem],
        out_specs=vmem,
        scratch_shapes=[pltpu.VMEM((SLOTS, 2 * BLOCK, BLOCK), jnp.float32)],
        compiler_params=pltpu.CompilerParams(vmem_limit_bytes=48 * 1024 * 1024),
        cost_estimate=pl.CostEstimate(flops=flops, transcendentals=0, bytes_accessed=11 * 1024 * 1024),
    )(ptab, qtab, slots_one, count_one, tiles, turned, model_one, kernel_u_one, kv_turned)


def _cos_sin(index, period):
    angles = index.astype(jnp.float32) * (TWO_PI / period)
    return jnp.cos(angles), jnp.sin(angles)


def channel_image(slot_grids, blocks_here):
    per_side = GRID // BLOCK
    grids = slot_grids.reshape(SLOTS, 2, BLOCK, BLOCK)
    block_rows = blocks_here // per_side
    block_cols = blocks_here % per_side
    offsets = jnp.arange(BLOCK, dtype=jnp.int32)
    pixel_rows = jnp.arange(ROWS, dtype=jnp.int32) - ROWS // 2
    er, ei = _cos_sin(jnp.mod(block_rows[:, None] * pixel_rows[None, :], PHASES), PHASES)
    br0, bi0 = _cos_sin(jnp.mod(pixel_rows[:, None] * (offsets - GRID // 2)[None, :], GRID), GRID)
    ar = er[:, :, None] * br0[None] - ei[:, :, None] * bi0[None]
    ai = er[:, :, None] * bi0[None] + ei[:, :, None] * br0[None]
    row_op = jnp.stack([jnp.stack([ar, -ai], axis=2), jnp.stack([ai, ar], axis=2)], axis=1)
    row_hi = row_op.astype(jnp.bfloat16)
    row_lo = (row_op - row_hi.astype(jnp.float32)).astype(jnp.bfloat16)
    rows_done = jnp.einsum("sclku,skuv->sclv", row_hi, grids, preferred_element_type=jnp.float32) + jnp.einsum(
        "sclku,skuv->sclv", row_lo, grids, preferred_element_type=jnp.float32
    )
    phases = jnp.arange(PHASES, dtype=jnp.int32)
    zr, zi = _cos_sin(jnp.mod(phases[:, None] * block_cols[None, :], PHASES), PHASES)
    phase_op = jnp.stack([jnp.stack([zr, -zi], axis=2), jnp.stack([zi, zr], axis=2)], axis=1)
    summed = jnp.einsum(
        "tcsk,sklv->ltcv", phase_op, rows_done, precision=lax.Precision.HIGH, preferred_element_type=jnp.float32
    )
    dr, di = _cos_sin(jnp.mod((phases[:, None] - GRID // 4) * offsets[None, :] - (GRID // 2) * phases[:, None], GRID), GRID)
    turned_r = summed[:, :, 0] * dr - summed[:, :, 1] * di
    turned_i = summed[:, :, 0] * di + summed[:, :, 1] * dr
    turned = jnp.concatenate([turned_r, turned_i], axis=2)
    col_groups = jnp.arange(CROP // PHASES, dtype=jnp.int32)
    gr, gi = _cos_sin(jnp.mod(offsets[:, None] * col_groups[None, :], BLOCK), BLOCK)
    col_op = jnp.concatenate([gr, -gi], axis=0)
    image = lax.dot_general(
        col_op,
        turned.reshape(ROWS * PHASES, 2 * BLOCK),
        (((0,), (1,)), ((), ())),
        precision=lax.Precision.HIGH,
        preferred_element_type=jnp.float32,
    )
    return (image * (1.0 / GRID)).reshape(CROP // PHASES, ROWS, PHASES)


def body(voltages, model_vis, kernel_u, kernel_v, pair_slot, slot_block, slot_count):
    local_antennas = voltages.shape[1]
    direct = voltages.reshape(voltages.shape[0], 1, local_antennas, 2 * SAMPLES)
    turned = lax.all_to_all(direct, ("grp", "chan"), split_axis=0, concat_axis=1, tiled=True)
    antenna_volts = turned.reshape(ANTENNAS, 2 * SAMPLES)
    slot_grids = grid_slots(
        antenna_volts, model_vis[0], kernel_u[0], kernel_v[0], pair_slot[0], slot_count
    )
    image_t = channel_image(slot_grids, slot_block[0])
    n_chan = lax.axis_size("chan")
    n_grp = lax.axis_size("grp")
    rows_per = ROWS // n_chan
    groups_per = CROP // PHASES // n_grp
    send = image_t.reshape(n_grp, groups_per, n_chan, rows_per * PHASES).transpose(0, 2, 1, 3)
    send = send.reshape(n_grp * n_chan, groups_per, rows_per * PHASES).astype(jnp.bfloat16)
    got = lax.all_to_all(send, ("grp", "chan"), split_axis=0, concat_axis=0, tiled=True)
    summed = got.astype(jnp.float32).sum(axis=0).reshape(groups_per, rows_per, PHASES)
    return summed.transpose(1, 0, 2).reshape(rows_per, groups_per * PHASES)


def solution(mesh):
    in_specs = (
        P(None, ("grp", "chan"), None),
        P(("grp", "chan"), None, None, None, None),
        P(("grp", "chan"), None, None, None),
        P(("grp", "chan"), None, None, None),
        P(("grp", "chan"), None),
        P(("grp", "chan"), None),
        P(("grp", "chan")),
    )
    out_specs = P("chan", "grp")
    return jax.shard_map(body, mesh=mesh, in_specs=in_specs, out_specs=out_specs, check_vma=False)
```
